1024 devices in a mesh: blk: 128 (over y, z_lo, core), uly: 8 (over x, z_hi).
Axes of the slice: x: 4, y: 4, z: 32 (z_hi: 2, z_lo: 16; z = z_hi * 16 + z_lo), core: 2. Of those that a mesh axis runs over, the one named last changes fastest.
Arguments:
- queries: bfloat16 [131072, 5120], P(('blk', 'uly')), may hold values from -6 to 6
- keys: bfloat16 [131072, 1024], P(('blk', 'uly')), may hold values from -6 to 6
- values: bfloat16 [131072, 1024], P(('blk', 'uly')), may hold values from -6 to 6
- document_lengths: int32 [257], replicated, may hold values from 1 to 1022, as said below
Outputs:
- attended: bfloat16 [131072, 5120], P(('blk', 'uly'))
The draws below stay inside these ranges and needn't reach their ends.
Inputs may be any that keep to these rules, and one draw needn't show every extreme that they name: `document_lengths`: the lengths sum to 131072; the largest is exactly 1022; every multiple of 1024 strictly between 0 and 131072 lies strictly inside a document.
All inputs are finite; a program needn't handle non-finite values.
Results may differ from the reference program's by a relative error of at most 0.0036.
Values may be sent and summed in bfloat16 or wider, within the bound.
No kernel may reach another device: no remote copies, remote signals or barrier semaphores. Data moves between devices by JAX's collectives and lax.ppermute only.
A program may use at most 64 MiB of HBM per device.

```python
import jax
import jax.numpy as jnp
from jax import lax

HQ = 40
KEY_VALUE_HEADS = 8
HEAD_SIZE = 128
DEVICE_TOKENS = 128
QUERY_PER_KEY = 5
BLOCK = 1024
PACKED_TOKENS = 131072
N_ULY = 8


def draw_queries(key, part):
    array_shape = (PACKED_TOKENS, HQ * HEAD_SIZE)
    base = jax.random.truncated_normal(jax.random.fold_in(key, 11), -6.0, 6.0, array_shape, jnp.float32)
    return base.astype(jnp.bfloat16)


def draw_keys(key, part):
    array_shape = (PACKED_TOKENS, KEY_VALUE_HEADS * HEAD_SIZE)
    base = jax.random.truncated_normal(jax.random.fold_in(key, 12), -6.0, 6.0, array_shape, jnp.float32)
    return base.astype(jnp.bfloat16)


def draw_document_lengths(key, part):
    runs = PACKED_TOKENS // BLOCK
    spans = jax.random.randint(jax.random.fold_in(key, 21), (runs + 1,), 2, BLOCK - 1, dtype=jnp.int32)
    before = jax.random.randint(jax.random.fold_in(key, 22), (runs + 1,), 1, spans, dtype=jnp.int32)
    after = (spans - before).astype(jnp.int32)
    after = after.at[0].set(1)
    limits = jnp.concatenate([jnp.full((1,), BLOCK - 1, jnp.int32), (BLOCK - 1 - after[:-1]).astype(jnp.int32)])
    before = jnp.minimum(before, limits).astype(jnp.int32)
    before = before.at[1].set(1)
    starts = jnp.arange(runs, dtype=jnp.int32) * BLOCK
    first_cut = after[:runs] + starts
    second_cut = BLOCK - before[1:] + starts
    cuts = jnp.stack([first_cut, second_cut], axis=1).reshape(-1)
    bounds = jnp.concatenate([jnp.zeros((1,), jnp.int32), cuts, jnp.full((1,), PACKED_TOKENS, jnp.int32)])
    return (bounds[1:] - bounds[:-1]).astype(jnp.int32)


def level_of(rng, dims, shards, least, largest):
    factor_of = 1.0
    for position, parts in shards:
        heights = jax.random.uniform(jax.random.fold_in(jax.random.fold_in(rng, 6), position), (parts,), jnp.float32, least / len(shards), largest / len(shards))
        factor_of = factor_of * jnp.repeat(jnp.exp(heights), dims[position] // parts).reshape((-1,) + (1,) * (len(dims) - 1 - position))
    return factor_of


def noise(key, shape, deviation, bound, pieces=(), held_as=jnp.bfloat16):
    drawn = deviation * jax.random.normal(key, shape, jnp.float32)
    if pieces:
        drawn = drawn * level_of(key, shape, pieces, -0.22, 0.18)
    return jnp.clip(drawn, -bound, bound).astype(held_as)


def setup_inputs(seed: int = 0) -> dict:
    arg_keys = jax.random.split(jax.random.key(seed), 5)
    return {
        "queries": draw_queries(jax.random.fold_in(arg_keys[4], 71), 0),
        "keys": draw_keys(jax.random.fold_in(arg_keys[4], 71), 0),
        "values": noise(arg_keys[2], (PACKED_TOKENS, KEY_VALUE_HEADS * HEAD_SIZE), 1.0, 6.0, ((0, 1024),)),
        "document_lengths": draw_document_lengths(jax.random.fold_in(arg_keys[4], 71), 0),
    }


NEGATIVE = -1.0e30


def document_of(places, ends):
    counted = jnp.sum((places[:, None] >= ends[None, :]).astype(jnp.int32), axis=1)
    return jnp.where(places >= 0, counted, -1).astype(jnp.int32)


def reference(queries, keys, values, document_lengths):
    ends = jnp.cumsum(document_lengths).astype(jnp.int32)
    backward_extent = N_ULY * DEVICE_TOKENS
    window_width = backward_extent + DEVICE_TOKENS
    keys_with_padding = jnp.concatenate([jnp.zeros((backward_extent, KEY_VALUE_HEADS * HEAD_SIZE), keys.dtype), keys], axis=0)
    values_with_padding = jnp.concatenate([jnp.zeros((backward_extent, KEY_VALUE_HEADS * HEAD_SIZE), values.dtype), values], axis=0)
    scale = float(HEAD_SIZE) ** -0.5

    def one_block(number):
        start_position = (number * DEVICE_TOKENS).astype(jnp.int32)
        query_rows = lax.dynamic_slice_in_dim(queries, start_position, DEVICE_TOKENS, 0).astype(jnp.float32).reshape(DEVICE_TOKENS, KEY_VALUE_HEADS, QUERY_PER_KEY, HEAD_SIZE)
        nearby_keys = lax.dynamic_slice_in_dim(keys_with_padding, start_position, window_width, 0).astype(jnp.float32).reshape(window_width, KEY_VALUE_HEADS, HEAD_SIZE)
        nearby_values = lax.dynamic_slice_in_dim(values_with_padding, start_position, window_width, 0).astype(jnp.float32).reshape(window_width, KEY_VALUE_HEADS, HEAD_SIZE)
        query_index = start_position + jnp.arange(DEVICE_TOKENS, dtype=jnp.int32)
        key_index = start_position - backward_extent + jnp.arange(window_width, dtype=jnp.int32)
        visible = (document_of(key_index, ends)[None, :] == document_of(query_index, ends)[:, None]) & (key_index[None, :] <= query_index[:, None])
        scores = jnp.einsum("thgd,whd->thgw", query_rows, nearby_keys) * scale
        mask = visible[:, None, None, :]
        top = jnp.max(jnp.where(mask, scores, NEGATIVE), axis=-1, keepdims=True)
        weight = jnp.where(mask, jnp.exp(scores - top), 0.0)
        total = jnp.sum(weight, axis=-1, keepdims=True)
        light = lax.optimization_barrier(weight.astype(jnp.bfloat16)).astype(jnp.float32)
        mixed = jnp.einsum("thgw,whd->thgd", light, nearby_values) / total
        return mixed.reshape(DEVICE_TOKENS, HQ * HEAD_SIZE).astype(jnp.bfloat16)

    blocks = lax.map(one_block, jnp.arange(PACKED_TOKENS // DEVICE_TOKENS, dtype=jnp.int32))
    return blocks.reshape(PACKED_TOKENS, HQ * HEAD_SIZE)
```

```python
import jax
import jax.numpy as jnp
from jax import lax
from jax.sharding import PartitionSpec as P

HEAD_SIZE = 128
QUERY_PER_KEY = 5


NEGATIVE = -1e30


def document_of(places, ends):
    counted = jnp.sum((places[:, None] >= ends[None, :]).astype(jnp.int32), axis=1)
    return jnp.where(places >= 0, counted, -1)


def attend(query_rows, nearby_keys, nearby_values, query_index, key_index, ends):
    count = query_rows.shape[0]
    window_width = nearby_keys.shape[0]
    heads = nearby_keys.shape[1] // HEAD_SIZE
    scale = float(HEAD_SIZE) ** (-0.5)
    grouped = jnp.moveaxis(query_rows.reshape(count, heads, QUERY_PER_KEY, HEAD_SIZE), 1, 0)
    key_heads = jnp.moveaxis(nearby_keys.reshape(window_width, heads, HEAD_SIZE), 1, 0)
    value_heads = jnp.moveaxis(nearby_values.reshape(window_width, heads, HEAD_SIZE), 1, 0)
    query_doc = document_of(query_index, ends)
    key_doc = document_of(key_index, ends)
    visible = (key_doc[None, :] == query_doc[:, None]) & (
        key_index[None, :] <= query_index[:, None]
    )
    mask = visible[:, None, :]

    def one_head(operands):
        query_head, key_head, value_head = operands
        scores = (
            jnp.einsum("tgd,wd->tgw", query_head, key_head, preferred_element_type=jnp.float32)
            * scale
        )
        top = jnp.max(jnp.where(mask, scores, NEGATIVE), axis=-1, keepdims=True)
        weight = jnp.where(mask, jnp.exp(scores - top), 0.0)
        total = jnp.sum(weight, axis=-1, keepdims=True)
        light = weight.astype(jnp.bfloat16)
        mixed = jnp.einsum("tgw,wd->tgd", light, value_head, preferred_element_type=jnp.float32)
        return mixed / total

    result = lax.map(one_head, (grouped, key_heads, value_heads))
    return (
        jnp.moveaxis(result, 0, 1)
        .reshape(count, heads * QUERY_PER_KEY * HEAD_SIZE)
        .astype(jnp.bfloat16)
    )


def plan(devices, back):
    crossing = [(f, f ^ 1) for f in range(devices)]
    slots = []
    for j in range(1, back + 1):
        pairs = []
        for d in range(devices):
            if d - j < 0:
                continue
            source = d - j if j % 2 == 0 else (d - j) ^ 1
            if source != d:
                pairs.append((source, d))
        slots.append(pairs)
    return crossing, slots


def on_device(queries, keys, values, document_lengths, *, crossing, slots):
    axes = ("blk", "uly")
    ends = jnp.cumsum(document_lengths)
    count = queries.shape[0]
    back = len(slots)
    flat = lax.axis_index("blk") * lax.axis_size("uly") + lax.axis_index("uly")
    cross_keys, cross_values = lax.ppermute((keys, values), axes, crossing)
    held_keys, held_values = [keys], [values]
    for j in range(1, back + 1):
        if j % 2 == 0:
            got = lax.ppermute((keys, values), axes, slots[j - 1])
        else:
            got = lax.ppermute((cross_keys, cross_values), axes, slots[j - 1])
            if j == 1:
                odd = (flat % 2) == 1
                got = (
                    jnp.where(odd, cross_keys, got[0]),
                    jnp.where(odd, cross_values, got[1]),
                )
        held_keys.append(got[0])
        held_values.append(got[1])
    nearby_keys = jnp.concatenate(held_keys[::-1], axis=0)
    nearby_values = jnp.concatenate(held_values[::-1], axis=0)
    start = flat * count
    query_index = start + jnp.arange(count, dtype=jnp.int32)
    key_index = start - back * count + jnp.arange((back + 1) * count, dtype=jnp.int32)
    return attend(queries, nearby_keys, nearby_values, query_index, key_index, ends)


def solution(mesh):
    devices = mesh.shape["blk"] * mesh.shape["uly"]
    crossing, slots = plan(devices, mesh.shape["uly"])
    placed = (P(("blk", "uly"), None), P(("blk", "uly"), None), P(("blk", "uly"), None), P())

    def body(queries, keys, values, document_lengths):
        return on_device(
            queries, keys, values, document_lengths, crossing=crossing, slots=slots
        )

    return jax.shard_map(
        body, mesh=mesh, in_specs=placed, out_specs=P(("blk", "uly"), None), check_vma=False
    )
```

```python
import jax
import jax.numpy as jnp
from jax import lax
from jax.sharding import PartitionSpec as P

HEAD_SIZE = 128
QUERY_PER_KEY = 5


NEGATIVE = -1e30


def document_of(places, ends):
    counted = jnp.sum((places[:, None] >= ends[None, :]).astype(jnp.int32), axis=1)
    return jnp.where(places >= 0, counted, -1)


def partial_attend(grouped, nearby, query_index, key_index, ends):
    window_width = nearby.shape[0]
    heads = grouped.shape[0]
    scale = float(HEAD_SIZE) ** (-0.5)
    width = heads * HEAD_SIZE
    key_heads = jnp.moveaxis(nearby[:, :width].reshape(window_width, heads, HEAD_SIZE), 1, 0)
    value_heads = jnp.moveaxis(nearby[:, width:].reshape(window_width, heads, HEAD_SIZE), 1, 0)
    query_doc = document_of(query_index, ends)
    key_doc = document_of(key_index, ends)
    visible = (key_doc[None, :] == query_doc[:, None]) & (
        key_index[None, :] <= query_index[:, None]
    )
    mask = visible[:, None, :]

    def one_head(operands):
        query_head, key_head, value_head = operands
        scores = (
            jnp.einsum("tgd,wd->tgw", query_head, key_head, preferred_element_type=jnp.float32)
            * scale
        )
        top = jnp.max(jnp.where(mask, scores, NEGATIVE), axis=-1, keepdims=True)
        weight = jnp.where(mask, jnp.exp(scores - top), 0.0)
        total = jnp.sum(weight, axis=-1, keepdims=True)
        light = weight.astype(jnp.bfloat16)
        mixed = jnp.einsum("tgw,wd->tgd", light, value_head, preferred_element_type=jnp.float32)
        return top, total, mixed

    return lax.map(one_head, (grouped, key_heads, value_heads))


def plan(devices, back):
    crossing = [(f, f ^ 1) for f in range(devices)]
    slots = []
    for j in range(1, back + 1):
        pairs = []
        for d in range(devices):
            if d - j < 0:
                continue
            source = d - j if j % 2 == 0 else (d - j) ^ 1
            if source != d:
                pairs.append((source, d))
        slots.append(pairs)
    return crossing, slots


def on_device(queries, keys, values, document_lengths, *, crossing, slots):
    axes = ("blk", "uly")
    ends = jnp.cumsum(document_lengths)
    count = queries.shape[0]
    back = len(slots)
    heads = keys.shape[1] // HEAD_SIZE
    flat = lax.axis_index("blk") * lax.axis_size("uly") + lax.axis_index("uly")
    joined = jnp.concatenate([keys, values], axis=1)
    crossed = lax.ppermute(joined, axes, crossing)
    held = {}
    for j in range(2, back + 1, 2):
        held[j] = lax.ppermute(joined, axes, slots[j - 1])
    for j in range(1, back + 1, 2):
        got = lax.ppermute(crossed, axes, slots[j - 1])
        if j == 1:
            got = jnp.where((flat % 2) == 1, crossed, got)
        held[j] = got
    start = flat * count
    query_index = start + jnp.arange(count, dtype=jnp.int32)
    grouped = jnp.moveaxis(queries.reshape(count, heads, QUERY_PER_KEY, HEAD_SIZE), 1, 0)

    def share(order, own):
        parts = [held[j] for j in order] + ([joined] if own else [])
        places = [start - j * count for j in order] + ([start] if own else [])
        key_index = jnp.concatenate(
            [p + jnp.arange(count, dtype=jnp.int32) for p in places]
        )
        return partial_attend(
            grouped, jnp.concatenate(parts, axis=0), query_index, key_index, ends
        )

    near_top, near_total, near_mixed = share(list(range(back, 0, -2)), True)
    far_top, far_total, far_mixed = share(list(range(back - 1, 0, -2)), False)
    top = jnp.maximum(near_top, far_top)
    near_scale = jnp.exp(near_top - top)
    far_scale = jnp.exp(far_top - top)
    total = near_total * near_scale + far_total * far_scale
    mixed = (near_mixed * near_scale + far_mixed * far_scale) / total
    return (
        jnp.moveaxis(mixed, 0, 1)
        .reshape(count, heads * QUERY_PER_KEY * HEAD_SIZE)
        .astype(jnp.bfloat16)
    )


def solution(mesh):
    devices = mesh.shape["blk"] * mesh.shape["uly"]
    crossing, slots = plan(devices, mesh.shape["uly"])
    placed = (P(("blk", "uly"), None), P(("blk", "uly"), None), P(("blk", "uly"), None), P())

    def body(queries, keys, values, document_lengths):
        return on_device(
            queries, keys, values, document_lengths, crossing=crossing, slots=slots
        )

    return jax.shard_map(
        body, mesh=mesh, in_specs=placed, out_specs=P(("blk", "uly"), None), check_vma=False
    )
```

```python
import jax
import jax.numpy as jnp
from jax import lax
from jax.sharding import PartitionSpec as P

HEAD_SIZE = 128
QUERY_PER_KEY = 5


NEGATIVE = -1e30
CHUNKS = 2


def document_of(places, ends):
    counted = jnp.sum((places[:, None] >= ends[None, :]).astype(jnp.int32), axis=1)
    return jnp.where(places >= 0, counted, -1)


def partial_attend(grouped, nearby, query_index, key_index, ends):
    window_width = nearby.shape[0]
    heads = grouped.shape[0]
    scale = float(HEAD_SIZE) ** (-0.5)
    width = heads * HEAD_SIZE
    key_heads = jnp.moveaxis(nearby[:, :width].reshape(window_width, heads, HEAD_SIZE), 1, 0)
    value_heads = jnp.moveaxis(nearby[:, width:].reshape(window_width, heads, HEAD_SIZE), 1, 0)
    query_doc = document_of(query_index, ends)
    key_doc = document_of(key_index, ends)
    visible = (key_doc[None, :] == query_doc[:, None]) & (
        key_index[None, :] <= query_index[:, None]
    )
    mask = visible[:, None, :]

    def one_head(operands):
        query_head, key_head, value_head = operands
        scores = (
            jnp.einsum("tgd,wd->tgw", query_head, key_head, preferred_element_type=jnp.float32)
            * scale
        )
        top = jnp.max(jnp.where(mask, scores, NEGATIVE), axis=-1, keepdims=True)
        weight = jnp.where(mask, jnp.exp(scores - top), 0.0)
        total = jnp.sum(weight, axis=-1, keepdims=True)
        light = weight.astype(jnp.bfloat16)
        mixed = jnp.einsum("tgw,wd->tgd", light, value_head, preferred_element_type=jnp.float32)
        return top, total, mixed

    return lax.map(one_head, (grouped, key_heads, value_heads))


def plan(devices, back):
    crossing = [(f, f ^ 1) for f in range(devices)]
    slots = []
    for j in range(1, back + 1):
        pairs = []
        for d in range(devices):
            if d - j < 0:
                continue
            source = d - j if j % 2 == 0 else (d - j) ^ 1
            if source != d:
                pairs.append((source, d))
        slots.append(pairs)
    return crossing, slots


def on_device(queries, keys, values, document_lengths, *, crossing, slots, chunks):
    axes = ("blk", "uly")
    ends = jnp.cumsum(document_lengths)
    count = queries.shape[0]
    back = len(slots)
    heads = keys.shape[1] // HEAD_SIZE
    group = heads // chunks
    flat = lax.axis_index("blk") * lax.axis_size("uly") + lax.axis_index("uly")
    odd = (flat % 2) == 1
    joined = jnp.concatenate([keys, values], axis=1)
    near = {j: lax.ppermute(joined, axes, slots[j - 1]) for j in range(2, back + 1, 2)}
    far = []
    previous = None
    for c in range(chunks):
        columns = slice(c * group * HEAD_SIZE, (c + 1) * group * HEAD_SIZE)
        piece = jnp.concatenate([keys[:, columns], values[:, columns]], axis=1)
        if previous is not None:
            previous, piece = lax.optimization_barrier((previous, piece))
        crossed = lax.ppermute(piece, axes, crossing)
        held = {}
        for j in range(1, back + 1, 2):
            got = lax.ppermute(crossed, axes, slots[j - 1])
            if j == 1:
                got = jnp.where(odd, crossed, got)
            held[j] = got
        far.append(held)
        previous = crossed
    start = flat * count
    query_index = start + jnp.arange(count, dtype=jnp.int32)
    grouped = jnp.moveaxis(queries.reshape(count, heads, QUERY_PER_KEY, HEAD_SIZE), 1, 0)

    def share(held, order, own, query_heads):
        parts = [held[j] for j in order] + ([joined] if own else [])
        places = [start - j * count for j in order] + ([start] if own else [])
        key_index = jnp.concatenate(
            [p + jnp.arange(count, dtype=jnp.int32) for p in places]
        )
        return partial_attend(
            query_heads, jnp.concatenate(parts, axis=0), query_index, key_index, ends
        )

    near_top, near_total, near_mixed = share(near, list(range(back, 0, -2)), True, grouped)
    pieces = [
        share(far[c], list(range(back - 1, 0, -2)), False, grouped[c * group:(c + 1) * group])
        for c in range(chunks)
    ]
    far_top, far_total, far_mixed = (
        jnp.concatenate([p[i] for p in pieces], axis=0) for i in range(3)
    )
    top = jnp.maximum(near_top, far_top)
    near_scale = jnp.exp(near_top - top)
    far_scale = jnp.exp(far_top - top)
    total = near_total * near_scale + far_total * far_scale
    mixed = (near_mixed * near_scale + far_mixed * far_scale) / total
    return (
        jnp.moveaxis(mixed, 0, 1)
        .reshape(count, heads * QUERY_PER_KEY * HEAD_SIZE)
        .astype(jnp.bfloat16)
    )


def solution(mesh):
    devices = mesh.shape["blk"] * mesh.shape["uly"]
    crossing, slots = plan(devices, mesh.shape["uly"])
    placed = (P(("blk", "uly"), None), P(("blk", "uly"), None), P(("blk", "uly"), None), P())

    def body(queries, keys, values, document_lengths):
        return on_device(
            queries, keys, values, document_lengths, crossing=crossing, slots=slots, chunks=CHUNKS
        )

    return jax.shard_map(
        body, mesh=mesh, in_specs=placed, out_specs=P(("blk", "uly"), None), check_vma=False
    )
```

```python
import jax
import jax.numpy as jnp
from jax import lax
from jax.sharding import PartitionSpec as P

HEAD_SIZE = 128
QUERY_PER_KEY = 5


NEGATIVE = -1e30


def document_of(places, ends):
    counted = jnp.sum((places[:, None] >= ends[None, :]).astype(jnp.int32), axis=1)
    return jnp.where(places >= 0, counted, -1)


def partial_attend(grouped, nearby, query_index, key_index, ends):
    window_width = nearby.shape[0]
    heads = grouped.shape[0]
    scale = float(HEAD_SIZE) ** (-0.5)
    width = heads * HEAD_SIZE
    key_heads = jnp.moveaxis(nearby[:, :width].reshape(window_width, heads, HEAD_SIZE), 1, 0)
    value_heads = jnp.moveaxis(nearby[:, width:].reshape(window_width, heads, HEAD_SIZE), 1, 0)
    query_doc = document_of(query_index, ends)
    key_doc = document_of(key_index, ends)
    visible = (key_doc[None, :] == query_doc[:, None]) & (
        key_index[None, :] <= query_index[:, None]
    )
    mask = visible[:, None, :]

    def one_head(operands):
        query_head, key_head, value_head = operands
        scores = (
            jnp.einsum("tgd,wd->tgw", query_head, key_head, preferred_element_type=jnp.float32)
            * scale
        )
        top = jnp.max(jnp.where(mask, scores, NEGATIVE), axis=-1, keepdims=True)
        weight = jnp.where(mask, jnp.exp(scores - top), 0.0)
        total = jnp.sum(weight, axis=-1, keepdims=True)
        light = weight.astype(jnp.bfloat16)
        mixed = jnp.einsum("tgw,wd->tgd", light, value_head, preferred_element_type=jnp.float32)
        return top, total, mixed

    return lax.map(one_head, (grouped, key_heads, value_heads))


def plan(devices, back):
    crossing = [(f, f ^ 1) for f in range(devices)]
    slots = []
    for j in range(1, back + 1):
        pairs = []
        for d in range(devices):
            if d - j < 0:
                continue
            source = d - j if j % 2 == 0 else (d - j) ^ 1
            if source != d:
                pairs.append((source, d))
        slots.append(pairs)
    return crossing, slots


def on_device(queries, keys, values, document_lengths, *, crossing, slots):
    axes = ("blk", "uly")
    ends = jnp.cumsum(document_lengths)
    count = queries.shape[0]
    back = len(slots)
    heads = keys.shape[1] // HEAD_SIZE
    flat = lax.axis_index("blk") * lax.axis_size("uly") + lax.axis_index("uly")
    joined = jnp.concatenate([keys, values], axis=1)
    crossed = lax.ppermute(joined, axes, crossing)
    held = {}
    for j in range(2, back + 1, 2):
        held[j] = lax.ppermute(joined, axes, slots[j - 1])
    start = flat * count
    query_index = start + jnp.arange(count, dtype=jnp.int32)
    grouped = jnp.moveaxis(queries.reshape(count, heads, QUERY_PER_KEY, HEAD_SIZE), 1, 0)

    def share(order, own):
        parts = [held[j] for j in order] + ([joined] if own else [])
        places = [start - j * count for j in order] + ([start] if own else [])
        key_index = jnp.concatenate(
            [p + jnp.arange(count, dtype=jnp.int32) for p in places]
        )
        return partial_attend(
            grouped, jnp.concatenate(parts, axis=0), query_index, key_index, ends
        )

    near_top, near_total, near_mixed = share(list(range(back, 0, -2)), True)
    near_top, crossed = lax.optimization_barrier((near_top, crossed))
    for j in range(1, back + 1, 2):
        got = lax.ppermute(crossed, axes, slots[j - 1])
        if j == 1:
            got = jnp.where((flat % 2) == 1, crossed, got)
        held[j] = got
    far_top, far_total, far_mixed = share(list(range(back - 1, 0, -2)), False)
    top = jnp.maximum(near_top, far_top)
    near_scale = jnp.exp(near_top - top)
    far_scale = jnp.exp(far_top - top)
    total = near_total * near_scale + far_total * far_scale
    mixed = (near_mixed * near_scale + far_mixed * far_scale) / total
    return (
        jnp.moveaxis(mixed, 0, 1)
        .reshape(count, heads * QUERY_PER_KEY * HEAD_SIZE)
        .astype(jnp.bfloat16)
    )


def solution(mesh):
    devices = mesh.shape["blk"] * mesh.shape["uly"]
    crossing, slots = plan(devices, mesh.shape["uly"])
    placed = (P(("blk", "uly"), None), P(("blk", "uly"), None), P(("blk", "uly"), None), P())

    def body(queries, keys, values, document_lengths):
        return on_device(
            queries, keys, values, document_lengths, crossing=crossing, slots=slots
        )

    return jax.shard_map(
        body, mesh=mesh, in_specs=placed, out_specs=P(("blk", "uly"), None), check_vma=False
    )
```

```python
import functools

import jax
import jax.numpy as jnp
from jax import lax
from jax.experimental import pallas as pl
from jax.sharding import PartitionSpec as P

HEAD_SIZE = 128
QUERY_PER_KEY = 5


NEGATIVE = -1e30


def document_of(places, ends):
    counted = jnp.sum((places[:, None] >= ends[None, :]).astype(jnp.int32), axis=1)
    return jnp.where(places >= 0, counted, -1)


def share_kernel(q_ref, k_ref, v_ref, qdoc_ref, qidx_ref, kdoc_ref, kidx_ref, top_ref, total_ref, mixed_ref, *, scale):
    scores = lax.dot_general(
        q_ref[0], k_ref[...], (((1,), (1,)), ((), ())), preferred_element_type=jnp.float32
    ) * scale
    visible = (kdoc_ref[...] == qdoc_ref[...]) & (kidx_ref[...] <= qidx_ref[...])
    top = jnp.max(jnp.where(visible, scores, NEGATIVE), axis=1, keepdims=True)
    weight = jnp.where(visible, jnp.exp(scores - top), 0.0)
    top_ref[0] = top
    total_ref[0] = jnp.sum(weight, axis=1, keepdims=True)
    mixed_ref[0] = jnp.dot(weight.astype(jnp.bfloat16), v_ref[...], preferred_element_type=jnp.float32)


def share_call(rows, nearby, row_doc, row_index, key_doc, key_index):
    heads, count, _ = rows.shape
    width = nearby.shape[0]
    kernel = functools.partial(share_kernel, scale=float(HEAD_SIZE) ** (-0.5))
    flops = 4 * heads * count * width * HEAD_SIZE
    return pl.pallas_call(
        kernel,
        grid=(heads,),
        in_specs=[
            pl.BlockSpec((1, count, HEAD_SIZE), lambda h: (h, 0, 0)),
            pl.BlockSpec((width, HEAD_SIZE), lambda h: (0, h)),
            pl.BlockSpec((width, HEAD_SIZE), lambda h: (0, heads + h)),
            pl.BlockSpec((count, 1), lambda h: (0, 0)),
            pl.BlockSpec((count, 1), lambda h: (0, 0)),
            pl.BlockSpec((1, width), lambda h: (0, 0)),
            pl.BlockSpec((1, width), lambda h: (0, 0)),
        ],
        out_specs=[
            pl.BlockSpec((1, count, 1), lambda h: (h, 0, 0)),
            pl.BlockSpec((1, count, 1), lambda h: (h, 0, 0)),
            pl.BlockSpec((1, count, HEAD_SIZE), lambda h: (h, 0, 0)),
        ],
        out_shape=[
            jax.ShapeDtypeStruct((heads, count, 1), jnp.float32),
            jax.ShapeDtypeStruct((heads, count, 1), jnp.float32),
            jax.ShapeDtypeStruct((heads, count, HEAD_SIZE), jnp.float32),
        ],
        cost_estimate=pl.CostEstimate(
            flops=flops, transcendentals=heads * count * width,
            bytes_accessed=2 * (rows.size + nearby.size) + 4 * heads * count * (HEAD_SIZE + 2),
        ),
    )(rows, nearby, nearby, row_doc, row_index, key_doc, key_index)


def plan(devices, back):
    crossing = [(f, f ^ 1) for f in range(devices)]
    slots = []
    for j in range(1, back + 1):
        pairs = []
        for d in range(devices):
            if d - j < 0:
                continue
            source = d - j if j % 2 == 0 else (d - j) ^ 1
            if source != d:
                pairs.append((source, d))
        slots.append(pairs)
    return crossing, slots


def on_device(queries, keys, values, document_lengths, *, crossing, slots):
    axes = ("blk", "uly")
    ends = jnp.cumsum(document_lengths)
    count = queries.shape[0]
    back = len(slots)
    heads = keys.shape[1] // HEAD_SIZE
    flat = lax.axis_index("blk") * lax.axis_size("uly") + lax.axis_index("uly")
    joined = jnp.concatenate([keys, values], axis=1)
    crossed = lax.ppermute(joined, axes, crossing)
    held = {}
    for j in range(2, back + 1, 2):
        held[j] = lax.ppermute(joined, axes, slots[j - 1])
    start = flat * count
    query_index = start + jnp.arange(count, dtype=jnp.int32)
    rows = jnp.moveaxis(queries.reshape(count, heads, QUERY_PER_KEY, HEAD_SIZE), 1, 0).reshape(
        heads, count * QUERY_PER_KEY, HEAD_SIZE
    )
    row_doc = jnp.repeat(document_of(query_index, ends), QUERY_PER_KEY)[:, None]
    row_index = jnp.repeat(query_index, QUERY_PER_KEY)[:, None]

    def share(order, own):
        parts = [held[j] for j in order] + ([joined] if own else [])
        places = [start - j * count for j in order] + ([start] if own else [])
        key_index = jnp.concatenate(
            [p + jnp.arange(count, dtype=jnp.int32) for p in places]
        )
        key_doc = document_of(key_index, ends)
        found = share_call(
            rows, jnp.concatenate(parts, axis=0), row_doc, row_index,
            key_doc[None, :], key_index[None, :],
        )
        return tuple(f.reshape(heads, count, QUERY_PER_KEY, f.shape[-1]) for f in found)

    near_top, near_total, near_mixed = share(list(range(back, 0, -2)), True)
    near_top, crossed = lax.optimization_barrier((near_top, crossed))
    for j in range(1, back + 1, 2):
        got = lax.ppermute(crossed, axes, slots[j - 1])
        if j == 1:
            got = jnp.where((flat % 2) == 1, crossed, got)
        held[j] = got
    far_top, far_total, far_mixed = share(list(range(back - 1, 0, -2)), False)
    top = jnp.maximum(near_top, far_top)
    near_scale = jnp.exp(near_top - top)
    far_scale = jnp.exp(far_top - top)
    total = near_total * near_scale + far_total * far_scale
    mixed = (near_mixed * near_scale + far_mixed * far_scale) / total
    return (
        jnp.moveaxis(mixed, 0, 1)
        .reshape(count, heads * QUERY_PER_KEY * HEAD_SIZE)
        .astype(jnp.bfloat16)
    )


def solution(mesh):
    devices = mesh.shape["blk"] * mesh.shape["uly"]
    crossing, slots = plan(devices, mesh.shape["uly"])
    placed = (P(("blk", "uly"), None), P(("blk", "uly"), None), P(("blk", "uly"), None), P())

    def body(queries, keys, values, document_lengths):
        return on_device(
            queries, keys, values, document_lengths, crossing=crossing, slots=slots
        )

    return jax.shard_map(
        body, mesh=mesh, in_specs=placed, out_specs=P(("blk", "uly"), None), check_vma=False
    )
```

```python
import functools

import jax
import jax.numpy as jnp
from jax import lax
from jax.experimental import pallas as pl
from jax.sharding import PartitionSpec as P

HEAD_SIZE = 128
QUERY_PER_KEY = 5


NEGATIVE = -1e30


def document_of(places, ends):
    counted = jnp.sum((places[:, None] >= ends[None, :]).astype(jnp.int32), axis=1)
    return jnp.where(places >= 0, counted, -1)


def share_kernel(q_ref, k_ref, v_ref, qdoc_ref, qidx_ref, kdoc_ref, kidx_ref, top_ref, total_ref, mixed_ref, *, scale):
    scores = lax.dot_general(
        q_ref[0], k_ref[...], (((1,), (1,)), ((), ())), preferred_element_type=jnp.float32
    ) * scale
    visible = (kdoc_ref[...] == qdoc_ref[...]) & (kidx_ref[...] <= qidx_ref[...])
    top = jnp.max(jnp.where(visible, scores, NEGATIVE), axis=1, keepdims=True)
    weight = jnp.where(visible, jnp.exp(scores - top), 0.0)
    top_ref[0] = top
    total_ref[0] = jnp.sum(weight, axis=1, keepdims=True)
    mixed_ref[0] = jnp.dot(weight.astype(jnp.bfloat16), v_ref[...], preferred_element_type=jnp.float32)


def share_call(rows, nearby, row_doc, row_index, key_doc, key_index):
    heads, count, _ = rows.shape
    width = nearby.shape[0]
    kernel = functools.partial(share_kernel, scale=float(HEAD_SIZE) ** (-0.5))
    flops = 4 * heads * count * width * HEAD_SIZE
    return pl.pallas_call(
        kernel,
        grid=(heads,),
        in_specs=[
            pl.BlockSpec((1, count, HEAD_SIZE), lambda h: (h, 0, 0)),
            pl.BlockSpec((width, HEAD_SIZE), lambda h: (0, h)),
            pl.BlockSpec((width, HEAD_SIZE), lambda h: (0, heads + h)),
            pl.BlockSpec((count, 1), lambda h: (0, 0)),
            pl.BlockSpec((count, 1), lambda h: (0, 0)),
            pl.BlockSpec((1, width), lambda h: (0, 0)),
            pl.BlockSpec((1, width), lambda h: (0, 0)),
        ],
        out_specs=[
            pl.BlockSpec((1, count, 1), lambda h: (h, 0, 0)),
            pl.BlockSpec((1, count, 1), lambda h: (h, 0, 0)),
            pl.BlockSpec((1, count, HEAD_SIZE), lambda h: (h, 0, 0)),
        ],
        out_shape=[
            jax.ShapeDtypeStruct((heads, count, 1), jnp.float32),
            jax.ShapeDtypeStruct((heads, count, 1), jnp.float32),
            jax.ShapeDtypeStruct((heads, count, HEAD_SIZE), jnp.float32),
        ],
        cost_estimate=pl.CostEstimate(
            flops=flops, transcendentals=heads * count * width,
            bytes_accessed=2 * (rows.size + nearby.size) + 4 * heads * count * (HEAD_SIZE + 2),
        ),
    )(rows, nearby, nearby, row_doc, row_index, key_doc, key_index)


def plan(devices, back):
    crossing = [(f, f ^ 1) for f in range(devices)]
    slots = []
    for j in range(1, back + 1):
        pairs = []
        for d in range(devices):
            if d - j < 0:
                continue
            source = d - j if j % 2 == 0 else (d - j) ^ 1
            if source != d:
                pairs.append((source, d))
        slots.append(pairs)
    return crossing, slots


def on_device(queries, keys, values, document_lengths, *, crossing, slots):
    axes = ("blk", "uly")
    ends = jnp.cumsum(document_lengths)
    count = queries.shape[0]
    back = len(slots)
    heads = keys.shape[1] // HEAD_SIZE
    flat = lax.axis_index("blk") * lax.axis_size("uly") + lax.axis_index("uly")
    joined = jnp.concatenate([keys, values], axis=1)
    held = {}
    for j in range(2, back + 1, 2):
        held[j] = lax.ppermute(joined, axes, slots[j - 1])
    *landed, sent = lax.optimization_barrier(tuple(held.values()) + (joined,))
    held = dict(zip(held.keys(), landed))
    crossed = lax.ppermute(sent, axes, crossing)
    start = flat * count
    query_index = start + jnp.arange(count, dtype=jnp.int32)
    rows = jnp.moveaxis(queries.reshape(count, heads, QUERY_PER_KEY, HEAD_SIZE), 1, 0).reshape(
        heads, count * QUERY_PER_KEY, HEAD_SIZE
    )
    row_doc = jnp.repeat(document_of(query_index, ends), QUERY_PER_KEY)[:, None]
    row_index = jnp.repeat(query_index, QUERY_PER_KEY)[:, None]

    def share(order, own):
        parts = [held[j] for j in order] + ([joined] if own else [])
        places = [start - j * count for j in order] + ([start] if own else [])
        key_index = jnp.concatenate(
            [p + jnp.arange(count, dtype=jnp.int32) for p in places]
        )
        key_doc = document_of(key_index, ends)
        found = share_call(
            rows, jnp.concatenate(parts, axis=0), row_doc, row_index,
            key_doc[None, :], key_index[None, :],
        )
        return tuple(f.reshape(heads, count, QUERY_PER_KEY, f.shape[-1]) for f in found)

    near_top, near_total, near_mixed = share(list(range(back, 0, -2)), True)
    near_top, crossed = lax.optimization_barrier((near_top, crossed))
    for j in range(1, back + 1, 2):
        got = lax.ppermute(crossed, axes, slots[j - 1])
        if j == 1:
            got = jnp.where((flat % 2) == 1, crossed, got)
        held[j] = got
    far_top, far_total, far_mixed = share(list(range(back - 1, 0, -2)), False)
    top = jnp.maximum(near_top, far_top)
    near_scale = jnp.exp(near_top - top)
    far_scale = jnp.exp(far_top - top)
    total = near_total * near_scale + far_total * far_scale
    mixed = (near_mixed * near_scale + far_mixed * far_scale) / total
    return (
        jnp.moveaxis(mixed, 0, 1)
        .reshape(count, heads * QUERY_PER_KEY * HEAD_SIZE)
        .astype(jnp.bfloat16)
    )


def solution(mesh):
    devices = mesh.shape["blk"] * mesh.shape["uly"]
    crossing, slots = plan(devices, mesh.shape["uly"])
    placed = (P(("blk", "uly"), None), P(("blk", "uly"), None), P(("blk", "uly"), None), P())

    def body(queries, keys, values, document_lengths):
        return on_device(
            queries, keys, values, document_lengths, crossing=crossing, slots=slots
        )

    return jax.shard_map(
        body, mesh=mesh, in_specs=placed, out_specs=P(("blk", "uly"), None), check_vma=False
    )
```

```python
import functools

import jax
import jax.numpy as jnp
from jax import lax
from jax.experimental import pallas as pl
from jax.sharding import PartitionSpec as P

HEAD_SIZE = 128
QUERY_PER_KEY = 5


NEGATIVE = -1e30


def document_of(places, ends):
    counted = jnp.sum((places[:, None] >= ends[None, :]).astype(jnp.int32), axis=1)
    return jnp.where(places >= 0, counted, -1)


def query_rows(q_ref):
    block = q_ref[...]
    return jnp.concatenate(
        [block[:, g * HEAD_SIZE:(g + 1) * HEAD_SIZE] for g in range(QUERY_PER_KEY)], axis=0
    )


def pieces(q_ref, k_ref, v_ref, qdoc_ref, qidx_ref, kdoc_ref, kidx_ref):
    scale = float(HEAD_SIZE) ** (-0.5)
    scores = lax.dot_general(
        query_rows(q_ref), k_ref[...], (((1,), (1,)), ((), ())),
        preferred_element_type=jnp.float32,
    ) * scale
    visible = (kdoc_ref[...] == qdoc_ref[...]) & (kidx_ref[...] <= qidx_ref[...])
    top = jnp.max(jnp.where(visible, scores, NEGATIVE), axis=1, keepdims=True)
    weight = jnp.where(visible, jnp.exp(scores - top), 0.0)
    total = jnp.sum(weight, axis=1, keepdims=True)
    mixed = jnp.dot(weight.astype(jnp.bfloat16), v_ref[...], preferred_element_type=jnp.float32)
    return top, total, mixed


def near_kernel(q_ref, k_ref, v_ref, qdoc_ref, qidx_ref, kdoc_ref, kidx_ref,
                top_ref, total_ref, mixed_ref):
    top, total, mixed = pieces(q_ref, k_ref, v_ref, qdoc_ref, qidx_ref, kdoc_ref, kidx_ref)
    top_ref[0] = top
    total_ref[0] = total
    mixed_ref[0] = mixed


def far_kernel(q_ref, k_ref, v_ref, qdoc_ref, qidx_ref, kdoc_ref, kidx_ref,
               ntop_ref, ntotal_ref, nmixed_ref, out_ref):
    far_top, far_total, far_mixed = pieces(
        q_ref, k_ref, v_ref, qdoc_ref, qidx_ref, kdoc_ref, kidx_ref
    )
    near_top = ntop_ref[0]
    top = jnp.maximum(near_top, far_top)
    near_scale = jnp.exp(near_top - top)
    far_scale = jnp.exp(far_top - top)
    total = ntotal_ref[0] * near_scale + far_total * far_scale
    mixed = (nmixed_ref[0] * near_scale + far_mixed * far_scale) / total
    count = out_ref.shape[0]
    for g in range(QUERY_PER_KEY):
        out_ref[:, g * HEAD_SIZE:(g + 1) * HEAD_SIZE] = (
            mixed[g * count:(g + 1) * count].astype(out_ref.dtype)
        )


def share_call(queries, nearby, row_doc, row_index, key_doc, key_index, near=None):
    count = queries.shape[0]
    width = nearby.shape[0]
    heads = nearby.shape[1] // (2 * HEAD_SIZE)
    rows = count * QUERY_PER_KEY
    span = QUERY_PER_KEY * HEAD_SIZE
    in_specs = [
        pl.BlockSpec((count, span), lambda h: (0, h)),
        pl.BlockSpec((width, HEAD_SIZE), lambda h: (0, h)),
        pl.BlockSpec((width, HEAD_SIZE), lambda h: (0, heads + h)),
        pl.BlockSpec((rows, 1), lambda h: (0, 0)),
        pl.BlockSpec((rows, 1), lambda h: (0, 0)),
        pl.BlockSpec((1, width), lambda h: (0, 0)),
        pl.BlockSpec((1, width), lambda h: (0, 0)),
    ]
    operands = [queries, nearby, nearby, row_doc, row_index, key_doc, key_index]
    piece_specs = [
        pl.BlockSpec((1, rows, 1), lambda h: (h, 0, 0)),
        pl.BlockSpec((1, rows, 1), lambda h: (h, 0, 0)),
        pl.BlockSpec((1, rows, HEAD_SIZE), lambda h: (h, 0, 0)),
    ]
    cost = pl.CostEstimate(
        flops=4 * heads * rows * width * HEAD_SIZE,
        transcendentals=heads * rows * width,
        bytes_accessed=2 * (queries.size + nearby.size) + 4 * heads * rows * (HEAD_SIZE + 2),
    )
    if near is None:
        return pl.pallas_call(
            near_kernel,
            grid=(heads,),
            in_specs=in_specs,
            out_specs=piece_specs,
            out_shape=[
                jax.ShapeDtypeStruct((heads, rows, 1), jnp.float32),
                jax.ShapeDtypeStruct((heads, rows, 1), jnp.float32),
                jax.ShapeDtypeStruct((heads, rows, HEAD_SIZE), jnp.float32),
            ],
            cost_estimate=cost,
        )(*operands)
    return pl.pallas_call(
        far_kernel,
        grid=(heads,),
        in_specs=in_specs + piece_specs,
        out_specs=pl.BlockSpec((count, span), lambda h: (0, h)),
        out_shape=jax.ShapeDtypeStruct(queries.shape, queries.dtype),
        cost_estimate=cost,
    )(*operands, *near)


def plan(devices, back):
    crossing = [(f, f ^ 1) for f in range(devices)]
    slots = []
    for j in range(1, back + 1):
        pairs = []
        for d in range(devices):
            if d - j < 0:
                continue
            source = d - j if j % 2 == 0 else (d - j) ^ 1
            if source != d:
                pairs.append((source, d))
        slots.append(pairs)
    return crossing, slots


def on_device(queries, keys, values, document_lengths, *, crossing, slots):
    axes = ("blk", "uly")
    ends = jnp.cumsum(document_lengths)
    count = queries.shape[0]
    back = len(slots)
    heads = keys.shape[1] // HEAD_SIZE
    flat = lax.axis_index("blk") * lax.axis_size("uly") + lax.axis_index("uly")
    joined = jnp.concatenate([keys, values], axis=1)
    held = {}
    for j in range(2, back + 1, 2):
        held[j] = lax.ppermute(joined, axes, slots[j - 1])
    *landed, sent = lax.optimization_barrier(tuple(held.values()) + (joined,))
    held = dict(zip(held.keys(), landed))
    crossed = lax.ppermute(sent, axes, crossing)
    start = flat * count
    query_index = start + jnp.arange(count, dtype=jnp.int32)
    query_doc = document_of(query_index, ends)
    row_doc = jnp.tile(query_doc, QUERY_PER_KEY)[:, None]
    row_index = jnp.tile(query_index, QUERY_PER_KEY)[:, None]

    def share(order, own, near=None):
        parts = [held[j] for j in order] + ([joined] if own else [])
        places = [start - j * count for j in order] + ([start] if own else [])
        key_index = jnp.concatenate(
            [p + jnp.arange(count, dtype=jnp.int32) for p in places]
        )
        key_doc = document_of(key_index, ends)
        return share_call(
            queries, jnp.concatenate(parts, axis=0), row_doc, row_index,
            key_doc[None, :], key_index[None, :], near,
        )

    near = share(list(range(back, 0, -2)), True)
    near, crossed = lax.optimization_barrier((near, crossed))
    for j in range(1, back + 1, 2):
        got = lax.ppermute(crossed, axes, slots[j - 1])
        if j == 1:
            got = jnp.where((flat % 2) == 1, crossed, got)
        held[j] = got
    return share(list(range(back - 1, 0, -2)), False, near)


def solution(mesh):
    devices = mesh.shape["blk"] * mesh.shape["uly"]
    crossing, slots = plan(devices, mesh.shape["uly"])
    placed = (P(("blk", "uly"), None), P(("blk", "uly"), None), P(("blk", "uly"), None), P())

    def body(queries, keys, values, document_lengths):
        return on_device(
            queries, keys, values, document_lengths, crossing=crossing, slots=slots
        )

    return jax.shard_map(
        body, mesh=mesh, in_specs=placed, out_specs=P(("blk", "uly"), None), check_vma=False
    )
```

```python
import functools

import jax
import jax.numpy as jnp
from jax import lax
from jax.experimental import pallas as pl
from jax.sharding import PartitionSpec as P

HEAD_SIZE = 128
QUERY_PER_KEY = 5


NEGATIVE = -1e30


def document_of(places, ends):
    counted = jnp.sum((places[:, None] >= ends[None, :]).astype(jnp.int32), axis=1)
    return jnp.where(places >= 0, counted, -1)


def query_rows(q_ref):
    block = q_ref[...]
    return jnp.concatenate(
        [block[:, g * HEAD_SIZE:(g + 1) * HEAD_SIZE] for g in range(QUERY_PER_KEY)], axis=0
    )


def pieces(q_ref, k_ref, v_ref, qdoc_ref, qidx_ref, kdoc_ref, kidx_ref):
    scale = float(HEAD_SIZE) ** (-0.5)
    scores = lax.dot_general(
        query_rows(q_ref), k_ref[...], (((1,), (1,)), ((), ())),
        preferred_element_type=jnp.float32,
    ) * scale
    visible = (kdoc_ref[...] == qdoc_ref[...]) & (kidx_ref[...] <= qidx_ref[...])
    top = jnp.max(jnp.where(visible, scores, NEGATIVE), axis=1, keepdims=True)
    weight = jnp.where(visible, jnp.exp(scores - top), 0.0)
    total = jnp.sum(weight, axis=1, keepdims=True)
    mixed = jnp.dot(weight.astype(jnp.bfloat16), v_ref[...], preferred_element_type=jnp.float32)
    return top, total, mixed


def near_kernel(q_ref, k_ref, v_ref, qdoc_ref, qidx_ref, kdoc_ref, kidx_ref,
                top_ref, total_ref, mixed_ref):
    top, total, mixed = pieces(q_ref, k_ref, v_ref, qdoc_ref, qidx_ref, kdoc_ref, kidx_ref)
    top_ref[0] = top
    total_ref[0] = total
    mixed_ref[0] = mixed


def far_kernel(q_ref, k_ref, v_ref, qdoc_ref, qidx_ref, kdoc_ref, kidx_ref,
               ntop_ref, ntotal_ref, nmixed_ref, out_ref):
    far_top, far_total, far_mixed = pieces(
        q_ref, k_ref, v_ref, qdoc_ref, qidx_ref, kdoc_ref, kidx_ref
    )
    near_top = ntop_ref[0]
    top = jnp.maximum(near_top, far_top)
    near_scale = jnp.exp(near_top - top)
    far_scale = jnp.exp(far_top - top)
    total = ntotal_ref[0] * near_scale + far_total * far_scale
    mixed = (nmixed_ref[0] * near_scale + far_mixed * far_scale) / total
    count = out_ref.shape[0]
    for g in range(QUERY_PER_KEY):
        out_ref[:, g * HEAD_SIZE:(g + 1) * HEAD_SIZE] = (
            mixed[g * count:(g + 1) * count].astype(out_ref.dtype)
        )


def share_call(queries, nearby, row_doc, row_index, key_doc, key_index, near=None):
    count = queries.shape[0]
    width = nearby.shape[0]
    heads = nearby.shape[1] // (2 * HEAD_SIZE)
    rows = count * QUERY_PER_KEY
    span = QUERY_PER_KEY * HEAD_SIZE
    in_specs = [
        pl.BlockSpec((count, span), lambda h: (0, h)),
        pl.BlockSpec((width, HEAD_SIZE), lambda h: (0, h)),
        pl.BlockSpec((width, HEAD_SIZE), lambda h: (0, heads + h)),
        pl.BlockSpec((rows, 1), lambda h: (0, 0)),
        pl.BlockSpec((rows, 1), lambda h: (0, 0)),
        pl.BlockSpec((1, width), lambda h: (0, 0)),
        pl.BlockSpec((1, width), lambda h: (0, 0)),
    ]
    operands = [queries, nearby, nearby, row_doc, row_index, key_doc, key_index]
    piece_specs = [
        pl.BlockSpec((1, rows, 1), lambda h: (h, 0, 0)),
        pl.BlockSpec((1, rows, 1), lambda h: (h, 0, 0)),
        pl.BlockSpec((1, rows, HEAD_SIZE), lambda h: (h, 0, 0)),
    ]
    cost = pl.CostEstimate(
        flops=4 * heads * rows * width * HEAD_SIZE,
        transcendentals=heads * rows * width,
        bytes_accessed=2 * (queries.size + nearby.size) + 4 * heads * rows * (HEAD_SIZE + 2),
    )
    if near is None:
        return pl.pallas_call(
            near_kernel,
            grid=(heads,),
            in_specs=in_specs,
            out_specs=piece_specs,
            out_shape=[
                jax.ShapeDtypeStruct((heads, rows, 1), jnp.float32),
                jax.ShapeDtypeStruct((heads, rows, 1), jnp.float32),
                jax.ShapeDtypeStruct((heads, rows, HEAD_SIZE), jnp.float32),
            ],
            cost_estimate=cost,
        )(*operands)
    return pl.pallas_call(
        far_kernel,
        grid=(heads,),
        in_specs=in_specs + piece_specs,
        out_specs=pl.BlockSpec((count, span), lambda h: (0, h)),
        out_shape=jax.ShapeDtypeStruct(queries.shape, queries.dtype),
        cost_estimate=cost,
    )(*operands, *near)


def plan(devices, back):
    crossing = [(f, f + 1) for f in range(devices - 1)]
    slots = {}
    for j in range(2, back + 1):
        pairs = []
        for d in range(devices):
            if d - j >= 0:
                pairs.append((d - j if j % 2 == 0 else d - j + 1, d))
        slots[j] = pairs
    return crossing, slots


def on_device(queries, keys, values, document_lengths, *, crossing, slots):
    axes = ("blk", "uly")
    ends = jnp.cumsum(document_lengths)
    count = queries.shape[0]
    back = max(slots)
    heads = keys.shape[1] // HEAD_SIZE
    flat = lax.axis_index("blk") * lax.axis_size("uly") + lax.axis_index("uly")
    joined = jnp.concatenate([keys, values], axis=1)
    held = {}
    for j in range(2, back + 1, 2):
        held[j] = lax.ppermute(joined, axes, slots[j])
    *landed, sent = lax.optimization_barrier(tuple(held.values()) + (joined,))
    held = dict(zip(held.keys(), landed))
    crossed = lax.ppermute(sent, axes, crossing)
    start = flat * count
    query_index = start + jnp.arange(count, dtype=jnp.int32)
    query_doc = document_of(query_index, ends)
    row_doc = jnp.tile(query_doc, QUERY_PER_KEY)[:, None]
    row_index = jnp.tile(query_index, QUERY_PER_KEY)[:, None]

    def share(order, own, near=None):
        parts = [held[j] for j in order] + ([joined] if own else [])
        places = [start - j * count for j in order] + ([start] if own else [])
        key_index = jnp.concatenate(
            [p + jnp.arange(count, dtype=jnp.int32) for p in places]
        )
        key_doc = document_of(key_index, ends)
        return share_call(
            queries, jnp.concatenate(parts, axis=0), row_doc, row_index,
            key_doc[None, :], key_index[None, :], near,
        )

    near = share(list(range(back, 0, -2)), True)
    near, crossed = lax.optimization_barrier((near, crossed))
    held[1] = crossed
    for j in range(3, back + 1, 2):
        held[j] = lax.ppermute(crossed, axes, slots[j])
    return share(list(range(back - 1, 0, -2)), False, near)


def solution(mesh):
    devices = mesh.shape["blk"] * mesh.shape["uly"]
    crossing, slots = plan(devices, mesh.shape["uly"])
    placed = (P(("blk", "uly"), None), P(("blk", "uly"), None), P(("blk", "uly"), None), P())

    def body(queries, keys, values, document_lengths):
        return on_device(
            queries, keys, values, document_lengths, crossing=crossing, slots=slots
        )

    return jax.shard_map(
        body, mesh=mesh, in_specs=placed, out_specs=P(("blk", "uly"), None), check_vma=False
    )
```

```python
import functools

import jax
import jax.numpy as jnp
from jax import lax
from jax.experimental import pallas as pl
from jax.sharding import PartitionSpec as P

HEAD_SIZE = 128
QUERY_PER_KEY = 5


NEGATIVE = -1e30
CHUNKS = 2


def document_of(places, ends):
    counted = jnp.sum((places[:, None] >= ends[None, :]).astype(jnp.int32), axis=1)
    return jnp.where(places >= 0, counted, -1)


def query_rows(q_ref):
    block = q_ref[...]
    return jnp.concatenate(
        [block[:, g * HEAD_SIZE:(g + 1) * HEAD_SIZE] for g in range(QUERY_PER_KEY)], axis=0
    )


def pieces(q_ref, k_ref, v_ref, qdoc_ref, qidx_ref, kdoc_ref, kidx_ref):
    scale = float(HEAD_SIZE) ** (-0.5)
    scores = lax.dot_general(
        query_rows(q_ref), k_ref[...], (((1,), (1,)), ((), ())),
        preferred_element_type=jnp.float32,
    ) * scale
    visible = (kdoc_ref[...] == qdoc_ref[...]) & (kidx_ref[...] <= qidx_ref[...])
    top = jnp.max(jnp.where(visible, scores, NEGATIVE), axis=1, keepdims=True)
    weight = jnp.where(visible, jnp.exp(scores - top), 0.0)
    total = jnp.sum(weight, axis=1, keepdims=True)
    mixed = jnp.dot(weight.astype(jnp.bfloat16), v_ref[...], preferred_element_type=jnp.float32)
    return top, total, mixed


def near_kernel(q_ref, k_ref, v_ref, qdoc_ref, qidx_ref, kdoc_ref, kidx_ref,
                top_ref, total_ref, mixed_ref):
    top, total, mixed = pieces(q_ref, k_ref, v_ref, qdoc_ref, qidx_ref, kdoc_ref, kidx_ref)
    top_ref[0] = top
    total_ref[0] = total
    mixed_ref[0] = mixed


def far_kernel(q_ref, k_ref, v_ref, qdoc_ref, qidx_ref, kdoc_ref, kidx_ref,
               ntop_ref, ntotal_ref, nmixed_ref, out_ref):
    far_top, far_total, far_mixed = pieces(
        q_ref, k_ref, v_ref, qdoc_ref, qidx_ref, kdoc_ref, kidx_ref
    )
    near_top = ntop_ref[0]
    top = jnp.maximum(near_top, far_top)
    near_scale = jnp.exp(near_top - top)
    far_scale = jnp.exp(far_top - top)
    total = ntotal_ref[0] * near_scale + far_total * far_scale
    mixed = (nmixed_ref[0] * near_scale + far_mixed * far_scale) / total
    count = out_ref.shape[0]
    for g in range(QUERY_PER_KEY):
        out_ref[:, g * HEAD_SIZE:(g + 1) * HEAD_SIZE] = (
            mixed[g * count:(g + 1) * count].astype(out_ref.dtype)
        )


def share_call(queries, nearby, row_doc, row_index, key_doc, key_index, near=None):
    count = queries.shape[0]
    width = nearby.shape[0]
    heads = nearby.shape[1] // (2 * HEAD_SIZE)
    rows = count * QUERY_PER_KEY
    span = QUERY_PER_KEY * HEAD_SIZE
    in_specs = [
        pl.BlockSpec((count, span), lambda h: (0, h)),
        pl.BlockSpec((width, HEAD_SIZE), lambda h: (0, h)),
        pl.BlockSpec((width, HEAD_SIZE), lambda h: (0, heads + h)),
        pl.BlockSpec((rows, 1), lambda h: (0, 0)),
        pl.BlockSpec((rows, 1), lambda h: (0, 0)),
        pl.BlockSpec((1, width), lambda h: (0, 0)),
        pl.BlockSpec((1, width), lambda h: (0, 0)),
    ]
    operands = [queries, nearby, nearby, row_doc, row_index, key_doc, key_index]
    piece_specs = [
        pl.BlockSpec((1, rows, 1), lambda h: (h, 0, 0)),
        pl.BlockSpec((1, rows, 1), lambda h: (h, 0, 0)),
        pl.BlockSpec((1, rows, HEAD_SIZE), lambda h: (h, 0, 0)),
    ]
    cost = pl.CostEstimate(
        flops=4 * heads * rows * width * HEAD_SIZE,
        transcendentals=heads * rows * width,
        bytes_accessed=2 * (queries.size + nearby.size) + 4 * heads * rows * (HEAD_SIZE + 2),
    )
    if near is None:
        return pl.pallas_call(
            near_kernel,
            grid=(heads,),
            in_specs=in_specs,
            out_specs=piece_specs,
            out_shape=[
                jax.ShapeDtypeStruct((heads, rows, 1), jnp.float32),
                jax.ShapeDtypeStruct((heads, rows, 1), jnp.float32),
                jax.ShapeDtypeStruct((heads, rows, HEAD_SIZE), jnp.float32),
            ],
            cost_estimate=cost,
        )(*operands)
    return pl.pallas_call(
        far_kernel,
        grid=(heads,),
        in_specs=in_specs + piece_specs,
        out_specs=pl.BlockSpec((count, span), lambda h: (0, h)),
        out_shape=jax.ShapeDtypeStruct(queries.shape, queries.dtype),
        cost_estimate=cost,
    )(*operands, *near)


def plan(devices, back):
    crossing = [(f, f ^ 1) for f in range(devices)]
    slots = []
    for j in range(1, back + 1):
        pairs = []
        for d in range(devices):
            if d - j < 0:
                continue
            source = d - j if j % 2 == 0 else (d - j) ^ 1
            if source != d:
                pairs.append((source, d))
        slots.append(pairs)
    return crossing, slots


def on_device(queries, keys, values, document_lengths, *, crossing, slots):
    axes = ("blk", "uly")
    ends = jnp.cumsum(document_lengths)
    count = queries.shape[0]
    back = len(slots)
    heads = keys.shape[1] // HEAD_SIZE
    flat = lax.axis_index("blk") * lax.axis_size("uly") + lax.axis_index("uly")
    joined = jnp.concatenate([keys, values], axis=1)
    held = {}
    for j in range(2, back + 1, 2):
        held[j] = lax.ppermute(joined, axes, slots[j - 1])
    *landed, keys, values = lax.optimization_barrier(tuple(held.values()) + (keys, values))
    held = dict(zip(held.keys(), landed))
    group = heads // CHUNKS
    pieces = []
    for c in range(CHUNKS):
        columns = slice(c * group * HEAD_SIZE, (c + 1) * group * HEAD_SIZE)
        pieces.append(jnp.concatenate([keys[:, columns], values[:, columns]], axis=1))
    crossed = lax.ppermute(pieces[0], axes, crossing)
    start = flat * count
    query_index = start + jnp.arange(count, dtype=jnp.int32)
    query_doc = document_of(query_index, ends)
    row_doc = jnp.tile(query_doc, QUERY_PER_KEY)[:, None]
    row_index = jnp.tile(query_index, QUERY_PER_KEY)[:, None]

    def share(held, order, own, near=None, heads_of=slice(None), window=None):
        parts = [held[j] for j in order] + ([window] if own else [])
        places = [start - j * count for j in order] + ([start] if own else [])
        key_index = jnp.concatenate(
            [p + jnp.arange(count, dtype=jnp.int32) for p in places]
        )
        key_doc = document_of(key_index, ends)
        span = QUERY_PER_KEY * HEAD_SIZE
        rows_of = queries if heads_of == slice(None) else queries[
            :, heads_of.start * span:heads_of.stop * span
        ]
        return share_call(
            rows_of, jnp.concatenate(parts, axis=0), row_doc, row_index,
            key_doc[None, :], key_index[None, :], near,
        )

    near = share(held, list(range(back, 0, -2)), True, window=joined)
    near, crossed = lax.optimization_barrier((near, crossed))
    outs = []
    for c in range(CHUNKS):
        if c + 1 < CHUNKS:
            crossed, following = lax.optimization_barrier((crossed, pieces[c + 1]))
            following = lax.ppermute(following, axes, crossing)
        far = {}
        for j in range(1, back + 1, 2):
            got = lax.ppermute(crossed, axes, slots[j - 1])
            if j == 1:
                got = jnp.where((flat % 2) == 1, crossed, got)
            far[j] = got
        part = slice(c * group, (c + 1) * group)
        outs.append(
            share(far, list(range(back - 1, 0, -2)), False,
                  tuple(n[part] for n in near), part)
        )
        if c + 1 < CHUNKS:
            crossed = following
    return jnp.concatenate(outs, axis=1)


def solution(mesh):
    devices = mesh.shape["blk"] * mesh.shape["uly"]
    crossing, slots = plan(devices, mesh.shape["uly"])
    placed = (P(("blk", "uly"), None), P(("blk", "uly"), None), P(("blk", "uly"), None), P())

    def body(queries, keys, values, document_lengths):
        return on_device(
            queries, keys, values, document_lengths, crossing=crossing, slots=slots
        )

    return jax.shard_map(
        body, mesh=mesh, in_specs=placed, out_specs=P(("blk", "uly"), None), check_vma=False
    )
```

```python
import functools

import jax
import jax.numpy as jnp
from jax import lax
from jax.experimental import pallas as pl
from jax.sharding import PartitionSpec as P

HEAD_SIZE = 128
QUERY_PER_KEY = 5


NEGATIVE = -1e30


def document_of(places, ends):
    counted = jnp.sum((places[:, None] >= ends[None, :]).astype(jnp.int32), axis=1)
    return jnp.where(places >= 0, counted, -1)


def query_rows(q_ref):
    block = q_ref[...]
    return jnp.concatenate(
        [block[:, g * HEAD_SIZE:(g + 1) * HEAD_SIZE] for g in range(QUERY_PER_KEY)], axis=0
    )


def pieces(q_ref, k_ref, v_ref, qdoc_ref, qidx_ref, kdoc_ref, kidx_ref):
    scale = float(HEAD_SIZE) ** (-0.5)
    scores = lax.dot_general(
        query_rows(q_ref), k_ref[...], (((1,), (1,)), ((), ())),
        preferred_element_type=jnp.float32,
    ) * scale
    visible = (kdoc_ref[...] == qdoc_ref[...]) & (kidx_ref[...] <= qidx_ref[...])
    top = jnp.max(jnp.where(visible, scores, NEGATIVE), axis=1, keepdims=True)
    weight = jnp.where(visible, jnp.exp(scores - top), 0.0)
    total = jnp.sum(weight, axis=1, keepdims=True)
    mixed = jnp.dot(weight.astype(jnp.bfloat16), v_ref[...], preferred_element_type=jnp.float32)
    return top, total, mixed


def near_kernel(q_ref, k_ref, v_ref, qdoc_ref, qidx_ref, kdoc_ref, kidx_ref,
                top_ref, total_ref, mixed_ref):
    top, total, mixed = pieces(q_ref, k_ref, v_ref, qdoc_ref, qidx_ref, kdoc_ref, kidx_ref)
    top_ref[0] = top
    total_ref[0] = total
    mixed_ref[0] = mixed


def far_kernel(q_ref, k_ref, v_ref, qdoc_ref, qidx_ref, kdoc_ref, kidx_ref,
               ntop_ref, ntotal_ref, nmixed_ref, out_ref):
    far_top, far_total, far_mixed = pieces(
        q_ref, k_ref, v_ref, qdoc_ref, qidx_ref, kdoc_ref, kidx_ref
    )
    near_top = ntop_ref[0]
    top = jnp.maximum(near_top, far_top)
    near_scale = jnp.exp(near_top - top)
    far_scale = jnp.exp(far_top - top)
    total = ntotal_ref[0] * near_scale + far_total * far_scale
    mixed = (nmixed_ref[0] * near_scale + far_mixed * far_scale) / total
    count = out_ref.shape[0]
    for g in range(QUERY_PER_KEY):
        out_ref[:, g * HEAD_SIZE:(g + 1) * HEAD_SIZE] = (
            mixed[g * count:(g + 1) * count].astype(out_ref.dtype)
        )


def share_call(queries, nearby, row_doc, row_index, key_doc, key_index, near=None):
    count = queries.shape[0]
    width = nearby.shape[0]
    heads = nearby.shape[1] // (2 * HEAD_SIZE)
    rows = count * QUERY_PER_KEY
    span = QUERY_PER_KEY * HEAD_SIZE
    in_specs = [
        pl.BlockSpec((count, span), lambda h: (0, h)),
        pl.BlockSpec((width, HEAD_SIZE), lambda h: (0, h)),
        pl.BlockSpec((width, HEAD_SIZE), lambda h: (0, heads + h)),
        pl.BlockSpec((rows, 1), lambda h: (0, 0)),
        pl.BlockSpec((rows, 1), lambda h: (0, 0)),
        pl.BlockSpec((1, width), lambda h: (0, 0)),
        pl.BlockSpec((1, width), lambda h: (0, 0)),
    ]
    operands = [queries, nearby, nearby, row_doc, row_index, key_doc, key_index]
    piece_specs = [
        pl.BlockSpec((1, rows, 1), lambda h: (h, 0, 0)),
        pl.BlockSpec((1, rows, 1), lambda h: (h, 0, 0)),
        pl.BlockSpec((1, rows, HEAD_SIZE), lambda h: (h, 0, 0)),
    ]
    cost = pl.CostEstimate(
        flops=4 * heads * rows * width * HEAD_SIZE,
        transcendentals=heads * rows * width,
        bytes_accessed=2 * (queries.size + nearby.size) + 4 * heads * rows * (HEAD_SIZE + 2),
    )
    if near is None:
        return pl.pallas_call(
            near_kernel,
            grid=(heads,),
            in_specs=in_specs,
            out_specs=piece_specs,
            out_shape=[
                jax.ShapeDtypeStruct((heads, rows, 1), jnp.float32),
                jax.ShapeDtypeStruct((heads, rows, 1), jnp.float32),
                jax.ShapeDtypeStruct((heads, rows, HEAD_SIZE), jnp.float32),
            ],
            cost_estimate=cost,
        )(*operands)
    return pl.pallas_call(
        far_kernel,
        grid=(heads,),
        in_specs=in_specs + piece_specs,
        out_specs=pl.BlockSpec((count, span), lambda h: (0, h)),
        out_shape=jax.ShapeDtypeStruct(queries.shape, queries.dtype),
        cost_estimate=cost,
    )(*operands, *near)


def plan(devices, back):
    crossing = [(f, f ^ 1) for f in range(devices)]
    slots = []
    for j in range(1, back + 1):
        pairs = []
        for d in range(devices):
            if d - j < 0:
                continue
            source = d - j if j % 2 == 0 else (d - j) ^ 1
            if source != d:
                pairs.append((source, d))
        slots.append(pairs)
    return crossing, slots


def on_device(queries, keys, values, document_lengths, *, crossing, slots):
    axes = ("blk", "uly")
    ends = jnp.cumsum(document_lengths)
    count = queries.shape[0]
    back = len(slots)
    heads = keys.shape[1] // HEAD_SIZE
    flat = lax.axis_index("blk") * lax.axis_size("uly") + lax.axis_index("uly")
    joined = jnp.concatenate([keys, values], axis=1)
    crossed = lax.ppermute(joined, axes, crossing)
    crossed, sent = lax.optimization_barrier((crossed, joined))
    held = {}
    for j in range(2, back + 1, 2):
        held[j] = lax.ppermute(sent, axes, slots[j - 1])
    start = flat * count
    query_index = start + jnp.arange(count, dtype=jnp.int32)
    query_doc = document_of(query_index, ends)
    row_doc = jnp.tile(query_doc, QUERY_PER_KEY)[:, None]
    row_index = jnp.tile(query_index, QUERY_PER_KEY)[:, None]

    def share(order, own, near=None):
        parts = [held[j] for j in order] + ([joined] if own else [])
        places = [start - j * count for j in order] + ([start] if own else [])
        key_index = jnp.concatenate(
            [p + jnp.arange(count, dtype=jnp.int32) for p in places]
        )
        key_doc = document_of(key_index, ends)
        return share_call(
            queries, jnp.concatenate(parts, axis=0), row_doc, row_index,
            key_doc[None, :], key_index[None, :], near,
        )

    near = share(list(range(back, 0, -2)), True)
    for j in range(1, back + 1, 2):
        got = lax.ppermute(crossed, axes, slots[j - 1])
        if j == 1:
            got = jnp.where((flat % 2) == 1, crossed, got)
        held[j] = got
    return share(list(range(back - 1, 0, -2)), False, near)


def solution(mesh):
    devices = mesh.shape["blk"] * mesh.shape["uly"]
    crossing, slots = plan(devices, mesh.shape["uly"])
    placed = (P(("blk", "uly"), None), P(("blk", "uly"), None), P(("blk", "uly"), None), P())

    def body(queries, keys, values, document_lengths):
        return on_device(
            queries, keys, values, document_lengths, crossing=crossing, slots=slots
        )

    return jax.shard_map(
        body, mesh=mesh, in_specs=placed, out_specs=P(("blk", "uly"), None), check_vma=False
    )
```

```python
import functools

import jax
import jax.numpy as jnp
from jax import lax
from jax.experimental import pallas as pl
from jax.sharding import PartitionSpec as P

HEAD_SIZE = 128
QUERY_PER_KEY = 5


NEGATIVE = -1e30


def document_of(places, ends):
    counted = jnp.sum((places[:, None] >= ends[None, :]).astype(jnp.int32), axis=1)
    return jnp.where(places >= 0, counted, -1)


def query_rows(q_ref):
    block = q_ref[...]
    return jnp.concatenate(
        [block[:, g * HEAD_SIZE:(g + 1) * HEAD_SIZE] for g in range(QUERY_PER_KEY)], axis=0
    )


def pieces(q_ref, k_ref, v_ref, qdoc_ref, qidx_ref, kdoc_ref, kidx_ref):
    scale = float(HEAD_SIZE) ** (-0.5)
    scores = lax.dot_general(
        query_rows(q_ref), k_ref[...], (((1,), (1,)), ((), ())),
        preferred_element_type=jnp.float32,
    ) * scale
    visible = (kdoc_ref[...] == qdoc_ref[...]) & (kidx_ref[...] <= qidx_ref[...])
    top = jnp.max(jnp.where(visible, scores, NEGATIVE), axis=1, keepdims=True)
    weight = jnp.where(visible, jnp.exp(scores - top), 0.0)
    total = jnp.sum(weight, axis=1, keepdims=True)
    mixed = jnp.dot(weight.astype(jnp.bfloat16), v_ref[...], preferred_element_type=jnp.float32)
    return top, total, mixed


def near_kernel(q_ref, k_ref, v_ref, qdoc_ref, qidx_ref, kdoc_ref, kidx_ref,
                top_ref, total_ref, mixed_ref):
    top, total, mixed = pieces(q_ref, k_ref, v_ref, qdoc_ref, qidx_ref, kdoc_ref, kidx_ref)
    top_ref[0] = top
    total_ref[0] = total
    mixed_ref[0] = mixed


def far_kernel(q_ref, k_ref, v_ref, qdoc_ref, qidx_ref, kdoc_ref, kidx_ref,
               ntop_ref, ntotal_ref, nmixed_ref, out_ref):
    far_top, far_total, far_mixed = pieces(
        q_ref, k_ref, v_ref, qdoc_ref, qidx_ref, kdoc_ref, kidx_ref
    )
    near_top = ntop_ref[0]
    top = jnp.maximum(near_top, far_top)
    near_scale = jnp.exp(near_top - top)
    far_scale = jnp.exp(far_top - top)
    total = ntotal_ref[0] * near_scale + far_total * far_scale
    mixed = (nmixed_ref[0] * near_scale + far_mixed * far_scale) / total
    count = out_ref.shape[0]
    for g in range(QUERY_PER_KEY):
        out_ref[:, g * HEAD_SIZE:(g + 1) * HEAD_SIZE] = (
            mixed[g * count:(g + 1) * count].astype(out_ref.dtype)
        )


def middle_kernel(q_ref, k_ref, v_ref, qdoc_ref, qidx_ref, kdoc_ref, kidx_ref,
                  ntop_ref, ntotal_ref, nmixed_ref, top_ref, total_ref, mixed_ref):
    far_top, far_total, far_mixed = pieces(
        q_ref, k_ref, v_ref, qdoc_ref, qidx_ref, kdoc_ref, kidx_ref
    )
    near_top = ntop_ref[0]
    top = jnp.maximum(near_top, far_top)
    near_scale = jnp.exp(near_top - top)
    far_scale = jnp.exp(far_top - top)
    top_ref[0] = top
    total_ref[0] = ntotal_ref[0] * near_scale + far_total * far_scale
    mixed_ref[0] = nmixed_ref[0] * near_scale + far_mixed * far_scale


def share_call(queries, nearby, row_doc, row_index, key_doc, key_index, near=None, last=True):
    count = queries.shape[0]
    width = nearby.shape[0]
    heads = nearby.shape[1] // (2 * HEAD_SIZE)
    rows = count * QUERY_PER_KEY
    span = QUERY_PER_KEY * HEAD_SIZE
    in_specs = [
        pl.BlockSpec((count, span), lambda h: (0, h)),
        pl.BlockSpec((width, HEAD_SIZE), lambda h: (0, h)),
        pl.BlockSpec((width, HEAD_SIZE), lambda h: (0, heads + h)),
        pl.BlockSpec((rows, 1), lambda h: (0, 0)),
        pl.BlockSpec((rows, 1), lambda h: (0, 0)),
        pl.BlockSpec((1, width), lambda h: (0, 0)),
        pl.BlockSpec((1, width), lambda h: (0, 0)),
    ]
    operands = [queries, nearby, nearby, row_doc, row_index, key_doc, key_index]
    piece_specs = [
        pl.BlockSpec((1, rows, 1), lambda h: (h, 0, 0)),
        pl.BlockSpec((1, rows, 1), lambda h: (h, 0, 0)),
        pl.BlockSpec((1, rows, HEAD_SIZE), lambda h: (h, 0, 0)),
    ]
    cost = pl.CostEstimate(
        flops=4 * heads * rows * width * HEAD_SIZE,
        transcendentals=heads * rows * width,
        bytes_accessed=2 * (queries.size + nearby.size) + 4 * heads * rows * (HEAD_SIZE + 2),
    )
    if near is None or not last:
        return pl.pallas_call(
            near_kernel if near is None else middle_kernel,
            grid=(heads,),
            in_specs=in_specs + ([] if near is None else piece_specs),
            out_specs=piece_specs,
            out_shape=[
                jax.ShapeDtypeStruct((heads, rows, 1), jnp.float32),
                jax.ShapeDtypeStruct((heads, rows, 1), jnp.float32),
                jax.ShapeDtypeStruct((heads, rows, HEAD_SIZE), jnp.float32),
            ],
            cost_estimate=cost,
        )(*operands, *([] if near is None else near))
    return pl.pallas_call(
        far_kernel,
        grid=(heads,),
        in_specs=in_specs + piece_specs,
        out_specs=pl.BlockSpec((count, span), lambda h: (0, h)),
        out_shape=jax.ShapeDtypeStruct(queries.shape, queries.dtype),
        cost_estimate=cost,
    )(*operands, *near)


def plan(devices, back):
    crossing = [(f, f ^ 1) for f in range(devices)]
    slots = []
    for j in range(1, back + 1):
        pairs = []
        for d in range(devices):
            if d - j < 0:
                continue
            source = d - j if j % 2 == 0 else (d - j) ^ 1
            if source != d:
                pairs.append((source, d))
        slots.append(pairs)
    return crossing, slots


def on_device(queries, keys, values, document_lengths, *, crossing, slots):
    axes = ("blk", "uly")
    ends = jnp.cumsum(document_lengths)
    count = queries.shape[0]
    back = len(slots)
    heads = keys.shape[1] // HEAD_SIZE
    flat = lax.axis_index("blk") * lax.axis_size("uly") + lax.axis_index("uly")
    joined = jnp.concatenate([keys, values], axis=1)
    held = {}
    for j in range(2, back + 1, 2):
        held[j] = lax.ppermute(joined, axes, slots[j - 1])
    *landed, sent = lax.optimization_barrier(tuple(held.values()) + (joined,))
    held = dict(zip(held.keys(), landed))
    crossed = lax.ppermute(sent, axes, crossing)
    start = flat * count
    query_index = start + jnp.arange(count, dtype=jnp.int32)
    query_doc = document_of(query_index, ends)
    row_doc = jnp.tile(query_doc, QUERY_PER_KEY)[:, None]
    row_index = jnp.tile(query_index, QUERY_PER_KEY)[:, None]

    def share(order, own, near=None, last=True):
        parts = [held[j] for j in order] + ([joined] if own else [])
        places = [start - j * count for j in order] + ([start] if own else [])
        key_index = jnp.concatenate(
            [p + jnp.arange(count, dtype=jnp.int32) for p in places]
        )
        key_doc = document_of(key_index, ends)
        return share_call(
            queries, jnp.concatenate(parts, axis=0), row_doc, row_index,
            key_doc[None, :], key_index[None, :], near, last,
        )

    near = share(list(range(back, 0, -2)), True)
    near, crossed = lax.optimization_barrier((near, crossed))
    for j in range(1, back + 1, 2):
        got = lax.ppermute(crossed, axes, slots[j - 1])
        if j == 1:
            got = jnp.where((flat % 2) == 1, crossed, got)
        held[j] = got
    near = share([back - 1, 1], False, near, last=False)
    return share(list(range(back - 3, 1, -2)), False, near)


def solution(mesh):
    devices = mesh.shape["blk"] * mesh.shape["uly"]
    crossing, slots = plan(devices, mesh.shape["uly"])
    placed = (P(("blk", "uly"), None), P(("blk", "uly"), None), P(("blk", "uly"), None), P())

    def body(queries, keys, values, document_lengths):
        return on_device(
            queries, keys, values, document_lengths, crossing=crossing, slots=slots
        )

    return jax.shard_map(
        body, mesh=mesh, in_specs=placed, out_specs=P(("blk", "uly"), None), check_vma=False
    )
```

```python
import functools

import jax
import jax.numpy as jnp
from jax import lax
from jax.experimental import pallas as pl
from jax.sharding import PartitionSpec as P

HEAD_SIZE = 128
QUERY_PER_KEY = 5


NEGATIVE = -1e30


def document_of(places, ends):
    counted = jnp.sum((places[:, None] >= ends[None, :]).astype(jnp.int32), axis=1)
    return jnp.where(places >= 0, counted, -1)


def query_rows(q_ref):
    block = q_ref[...]
    return jnp.concatenate(
        [block[:, g * HEAD_SIZE:(g + 1) * HEAD_SIZE] for g in range(QUERY_PER_KEY)], axis=0
    )


def pieces(q_ref, k_ref, v_ref, qdoc_ref, qidx_ref, kdoc_ref, kidx_ref):
    scale = float(HEAD_SIZE) ** (-0.5)
    scores = lax.dot_general(
        query_rows(q_ref), k_ref[...], (((1,), (1,)), ((), ())),
        preferred_element_type=jnp.float32,
    ) * scale
    visible = (kdoc_ref[...] == qdoc_ref[...]) & (kidx_ref[...] <= qidx_ref[...])
    top = jnp.max(jnp.where(visible, scores, NEGATIVE), axis=1, keepdims=True)
    weight = jnp.where(visible, jnp.exp(scores - top), 0.0)
    total = jnp.sum(weight, axis=1, keepdims=True)
    mixed = jnp.dot(weight.astype(jnp.bfloat16), v_ref[...], preferred_element_type=jnp.float32)
    return top, total, mixed


def near_kernel(q_ref, k_ref, v_ref, qdoc_ref, qidx_ref, kdoc_ref, kidx_ref,
                top_ref, total_ref, mixed_ref):
    top, total, mixed = pieces(q_ref, k_ref, v_ref, qdoc_ref, qidx_ref, kdoc_ref, kidx_ref)
    top_ref[0] = top
    total_ref[0] = total
    mixed_ref[0] = mixed


def far_kernel(q_ref, k_ref, v_ref, qdoc_ref, qidx_ref, kdoc_ref, kidx_ref,
               ntop_ref, ntotal_ref, nmixed_ref, out_ref):
    far_top, far_total, far_mixed = pieces(
        q_ref, k_ref, v_ref, qdoc_ref, qidx_ref, kdoc_ref, kidx_ref
    )
    near_top = ntop_ref[0]
    top = jnp.maximum(near_top, far_top)
    near_scale = jnp.exp(near_top - top)
    far_scale = jnp.exp(far_top - top)
    total = ntotal_ref[0] * near_scale + far_total * far_scale
    mixed = (nmixed_ref[0] * near_scale + far_mixed * far_scale) / total
    count = out_ref.shape[0]
    for g in range(QUERY_PER_KEY):
        out_ref[:, g * HEAD_SIZE:(g + 1) * HEAD_SIZE] = (
            mixed[g * count:(g + 1) * count].astype(out_ref.dtype)
        )


def middle_kernel(q_ref, k_ref, v_ref, qdoc_ref, qidx_ref, kdoc_ref, kidx_ref,
                  ntop_ref, ntotal_ref, nmixed_ref, top_ref, total_ref, mixed_ref):
    far_top, far_total, far_mixed = pieces(
        q_ref, k_ref, v_ref, qdoc_ref, qidx_ref, kdoc_ref, kidx_ref
    )
    near_top = ntop_ref[0]
    top = jnp.maximum(near_top, far_top)
    near_scale = jnp.exp(near_top - top)
    far_scale = jnp.exp(far_top - top)
    top_ref[0] = top
    total_ref[0] = ntotal_ref[0] * near_scale + far_total * far_scale
    mixed_ref[0] = nmixed_ref[0] * near_scale + far_mixed * far_scale


def share_call(queries, nearby, row_doc, row_index, key_doc, key_index, near=None, last=True):
    count = queries.shape[0]
    width = nearby.shape[0]
    heads = nearby.shape[1] // (2 * HEAD_SIZE)
    rows = count * QUERY_PER_KEY
    span = QUERY_PER_KEY * HEAD_SIZE
    in_specs = [
        pl.BlockSpec((count, span), lambda h: (0, h)),
        pl.BlockSpec((width, HEAD_SIZE), lambda h: (0, h)),
        pl.BlockSpec((width, HEAD_SIZE), lambda h: (0, heads + h)),
        pl.BlockSpec((rows, 1), lambda h: (0, 0)),
        pl.BlockSpec((rows, 1), lambda h: (0, 0)),
        pl.BlockSpec((1, width), lambda h: (0, 0)),
        pl.BlockSpec((1, width), lambda h: (0, 0)),
    ]
    operands = [queries, nearby, nearby, row_doc, row_index, key_doc, key_index]
    piece_specs = [
        pl.BlockSpec((1, rows, 1), lambda h: (h, 0, 0)),
        pl.BlockSpec((1, rows, 1), lambda h: (h, 0, 0)),
        pl.BlockSpec((1, rows, HEAD_SIZE), lambda h: (h, 0, 0)),
    ]
    cost = pl.CostEstimate(
        flops=4 * heads * rows * width * HEAD_SIZE,
        transcendentals=heads * rows * width,
        bytes_accessed=2 * (queries.size + nearby.size) + 4 * heads * rows * (HEAD_SIZE + 2),
    )
    if near is None or not last:
        return pl.pallas_call(
            near_kernel if near is None else middle_kernel,
            grid=(heads,),
            in_specs=in_specs + ([] if near is None else piece_specs),
            out_specs=piece_specs,
            out_shape=[
                jax.ShapeDtypeStruct((heads, rows, 1), jnp.float32),
                jax.ShapeDtypeStruct((heads, rows, 1), jnp.float32),
                jax.ShapeDtypeStruct((heads, rows, HEAD_SIZE), jnp.float32),
            ],
            cost_estimate=cost,
        )(*operands, *([] if near is None else near))
    return pl.pallas_call(
        far_kernel,
        grid=(heads,),
        in_specs=in_specs + piece_specs,
        out_specs=pl.BlockSpec((count, span), lambda h: (0, h)),
        out_shape=jax.ShapeDtypeStruct(queries.shape, queries.dtype),
        cost_estimate=cost,
    )(*operands, *near)


def plan(devices, back):
    crossing = [(f, f ^ 1) for f in range(devices)]
    slots = []
    for j in range(1, back + 1):
        pairs = []
        for d in range(devices):
            if d - j < 0:
                continue
            source = d - j if j % 2 == 0 else (d - j) ^ 1
            if source != d:
                pairs.append((source, d))
        slots.append(pairs)
    return crossing, slots


def on_device(queries, keys, values, document_lengths, *, crossing, slots):
    axes = ("blk", "uly")
    ends = jnp.cumsum(document_lengths)
    count = queries.shape[0]
    back = len(slots)
    heads = keys.shape[1] // HEAD_SIZE
    flat = lax.axis_index("blk") * lax.axis_size("uly") + lax.axis_index("uly")
    joined = jnp.concatenate([keys, values], axis=1)
    held = {}
    for j in range(2, back + 1, 2):
        held[j] = lax.ppermute(joined, axes, slots[j - 1])
    *landed, sent = lax.optimization_barrier(tuple(held.values()) + (joined,))
    held = dict(zip(held.keys(), landed))
    crossed = lax.ppermute(sent, axes, crossing)
    start = flat * count
    query_index = start + jnp.arange(count, dtype=jnp.int32)
    query_doc = document_of(query_index, ends)
    row_doc = jnp.tile(query_doc, QUERY_PER_KEY)[:, None]
    row_index = jnp.tile(query_index, QUERY_PER_KEY)[:, None]

    def share(order, own, near=None, last=True):
        parts = [held[j] for j in order] + ([joined] if own else [])
        places = [start - j * count for j in order] + ([start] if own else [])
        key_index = jnp.concatenate(
            [p + jnp.arange(count, dtype=jnp.int32) for p in places]
        )
        key_doc = document_of(key_index, ends)
        return share_call(
            queries, jnp.concatenate(parts, axis=0), row_doc, row_index,
            key_doc[None, :], key_index[None, :], near, last,
        )

    near = share(list(range(back, 0, -2)), True)
    near, crossed = lax.optimization_barrier((near, crossed))
    for j in range(1, back + 1, 2):
        got = lax.ppermute(crossed, axes, slots[j - 1])
        if j == 1:
            got = jnp.where((flat % 2) == 1, crossed, got)
        held[j] = got
    near = share([back - 1, 1], False, near, last=False)
    for j in range(back - 3, 3, -2):
        near = share([j], False, near, last=False)
    return share([3], False, near)


def solution(mesh):
    devices = mesh.shape["blk"] * mesh.shape["uly"]
    crossing, slots = plan(devices, mesh.shape["uly"])
    placed = (P(("blk", "uly"), None), P(("blk", "uly"), None), P(("blk", "uly"), None), P())

    def body(queries, keys, values, document_lengths):
        return on_device(
            queries, keys, values, document_lengths, crossing=crossing, slots=slots
        )

    return jax.shard_map(
        body, mesh=mesh, in_specs=placed, out_specs=P(("blk", "uly"), None), check_vma=False
    )
```
